256 devices in a mesh: space: 64 (over x, y, z_hi), chan: 4 (over z_lo, core).
Axes of the slice: x: 4, y: 4, z: 8 (z_hi: 4, z_lo: 2; z = z_hi * 2 + z_lo), core: 2. Of those that a mesh axis runs over, the one named last changes fastest.
Arguments:
- voxels: bfloat16 [32, 128, 16, 512], P(None, 'space'), may hold values from -6 to 6
- first_filters: bfloat16 [3, 3, 3, 64, 32], P(None, None, None, 'chan'), may hold values from -0.21875 to 0.21875
- second_filters: bfloat16 [3, 3, 3, 64, 64], P(None, None, None, 'chan'), may hold values from -0.15625 to 0.15625
Outputs:
- filtered: bfloat16 [64, 128, 16, 512], P('chan', 'space')
The draws below stay inside these ranges and needn't reach their ends.
All inputs are finite; a program needn't handle non-finite values.
Results may differ from the reference program's by a relative error of at most 0.0049.
Values may be sent and summed in bfloat16 or wider, within the bound.
No kernel may reach another device: no remote copies, remote signals or barrier semaphores. Data moves between devices by JAX's collectives and lax.ppermute only.
A program may use at most 64 MiB of HBM per device.

```python
import jax
import jax.numpy as jnp
from jax import lax

C_IN = 32
C_MID = 64
C_OUT = 64
GH = 8
TD = 2
TH = 16
W = 512
TILE_ROWS = 128
N_SPACE = 64


def block_scale(own_key, dims, cuts, smallest, high):
    def one(position, parts):
        steps = jax.random.uniform(jax.random.fold_in(jax.random.fold_in(own_key, 6), position), (parts,), jnp.float32, smallest / len(cuts), high / len(cuts))
        return jnp.repeat(jnp.exp(steps), dims[position] // parts).reshape((-1,) + (1,) * (len(dims) - position - 1))

    level = one(*cuts[0])
    for cut in cuts[1:]:
        level = level * one(*cut)
    return level


def scatter_about(key, extent, width, bound, shards=(), dtype=jnp.bfloat16):
    gain = block_scale(key, extent, shards, -0.22, 0.18) if shards else 1.0
    drawn = jax.random.normal(key, extent, jnp.float32) * width * gain
    return jnp.minimum(jnp.maximum(drawn, -bound), bound).astype(dtype)


def setup_inputs(seed: int = 0) -> dict:
    key_list = jax.random.split(jax.random.key(seed), 4)
    return {
        "voxels": scatter_about(key_list[0], (C_IN, TILE_ROWS, TH, W), 1.0, 6.0, ((1, 64),)),
        "first_filters": scatter_about(key_list[1], (3, 3, 3, C_MID, C_IN), (27 * C_IN) ** -0.5, 0.21875, ((3, 4),)),
        "second_filters": scatter_about(key_list[2], (3, 3, 3, C_OUT, C_MID), (27 * C_MID) ** -0.5, 0.15625, ((3, 4),)),
    }


def to_volume(tile_array):
    channels = tile_array.shape[0]
    grid_depth = N_SPACE // GH
    shaped = tile_array.reshape(channels, N_SPACE, TD, TH, W)
    shaped = jnp.roll(shaped, GH + GH // 4, axis=1)
    shaped = shaped.reshape(channels, grid_depth, GH, TD, TH, W)
    shaped = shaped.transpose(0, 1, 3, 2, 4, 5)
    return shaped.reshape(channels, grid_depth * TD, GH * TH, W)


def to_tiles(volume):
    channels = volume.shape[0]
    grid_depth = N_SPACE // GH
    shaped = volume.reshape(channels, grid_depth, TD, GH, TH, W)
    shaped = shaped.transpose(0, 1, 3, 2, 4, 5)
    shaped = shaped.reshape(channels, N_SPACE, TD, TH, W)
    shaped = jnp.roll(shaped, -(GH + GH // 4), axis=1)
    return shaped.reshape(channels, N_SPACE * TD, TH, W)


def correlate(volume, filters):
    kernel = filters.astype(jnp.float32).transpose(3, 4, 0, 1, 2)
    result = lax.conv_general_dilated(volume.astype(jnp.float32)[None], kernel, (1, 1, 1), "SAME",
                                      dimension_numbers=("NCDHW", "OIDHW", "NCDHW"))
    return result[0]


def reference(voxels, first_filters, second_filters):
    volume = to_volume(voxels)
    hidden = jax.nn.relu(correlate(volume, first_filters)).astype(jnp.bfloat16)
    output = jax.nn.relu(correlate(hidden, second_filters)).astype(jnp.bfloat16)
    return to_tiles(output)
```

```python
import jax
import jax.numpy as jnp
from jax import lax
from jax.sharding import PartitionSpec as P

GH = 8


def passed_along(value, axis, steps):
    count = lax.axis_size(axis)
    pairs = [(source, (source + steps) % count) for source in range(count)]
    return lax.ppermute(value, axis, pairs)


def tile_place():
    tile_count = lax.axis_size("space")
    position = (lax.axis_index("space") + GH + GH // 4) % tile_count
    return position % GH, position // GH, tile_count // GH


def wide_border(volume_tile, rim):
    tile_row, depth_tile, grid_depth = tile_place()
    above_rim = passed_along(volume_tile[:, :, -rim:, :], "space", 1)
    below_rim = passed_along(volume_tile[:, :, :rim, :], "space", -1)
    above_rim = jnp.where(tile_row > 0, above_rim, jnp.zeros_like(above_rim))
    below_rim = jnp.where(tile_row < GH - 1, below_rim, jnp.zeros_like(below_rim))
    taller = jnp.concatenate([above_rim, volume_tile, below_rim], 2)
    front_rim = passed_along(taller[:, -rim:], "space", GH)
    back_rim = passed_along(taller[:, :rim], "space", -GH)
    front_rim = jnp.where(depth_tile > 0, front_rim, jnp.zeros_like(front_rim))
    back_rim = jnp.where(depth_tile < grid_depth - 1, back_rim, jnp.zeros_like(back_rim))
    return jnp.concatenate([front_rim, taller, back_rim], 1)


def conv_valid(stacked, filters):
    kernel = filters.transpose(3, 4, 0, 1, 2)
    result = lax.conv_general_dilated(
        stacked[None], kernel, (1, 1, 1), ((0, 0), (0, 0), (1, 1)),
        dimension_numbers=("NCDHW", "OIDHW", "NCDHW"), preferred_element_type=jnp.float32)
    return result[0]


def inside_mask(depth_rows, height_rows):
    tile_row, depth_tile, grid_depth = tile_place()
    d = lax.broadcasted_iota(jnp.int32, (depth_rows, height_rows, 1), 0)
    h = lax.broadcasted_iota(jnp.int32, (depth_rows, height_rows, 1), 1)
    keep = (d > 0) | (depth_tile > 0)
    keep &= (d < depth_rows - 1) | (depth_tile < grid_depth - 1)
    keep &= (h > 0) | (tile_row > 0)
    keep &= (h < height_rows - 1) | (tile_row < GH - 1)
    return keep


def local(voxels, first_filters, second_filters):
    all_first = lax.all_gather(first_filters, "chan", axis=3, tiled=True)
    padded = wide_border(voxels, 2)
    hidden = jax.nn.relu(conv_valid(padded, all_first))
    keep = inside_mask(hidden.shape[1], hidden.shape[2])
    hidden = jnp.where(keep[None], hidden, 0.0).astype(jnp.bfloat16)
    summed = conv_valid(hidden, second_filters)
    return jax.nn.relu(summed).astype(jnp.bfloat16)


def solution(mesh):
    return jax.shard_map(
        local,
        mesh=mesh,
        in_specs=(
            P(None, "space", None, None),
            P(None, None, None, "chan", None),
            P(None, None, None, "chan", None),
        ),
        out_specs=P("chan", "space", None, None),
        check_vma=False,
    )
```

```python
import functools

import jax
import jax.numpy as jnp
from jax import lax
from jax.experimental import pallas as pl
from jax.experimental.pallas import tpu as pltpu
from jax.sharding import PartitionSpec as P

GH = 8


def passed_along(value, axis, steps):
    count = lax.axis_size(axis)
    pairs = [(source, (source + steps) % count) for source in range(count)]
    return lax.ppermute(value, axis, pairs)


def tile_place():
    tile_count = lax.axis_size("space")
    position = (lax.axis_index("space") + GH + GH // 4) % tile_count
    return position % GH, position // GH, tile_count // GH


def wide_border(volume_tile, rim):
    tile_row, depth_tile, grid_depth = tile_place()
    above_rim = passed_along(volume_tile[:, -rim:], "space", 1)
    below_rim = passed_along(volume_tile[:, :rim], "space", -1)
    above_rim = jnp.where(tile_row > 0, above_rim, jnp.zeros_like(above_rim))
    below_rim = jnp.where(tile_row < GH - 1, below_rim, jnp.zeros_like(below_rim))
    taller = jnp.concatenate([above_rim, volume_tile, below_rim], 1)
    front_rim = passed_along(taller[-rim:], "space", GH)
    back_rim = passed_along(taller[:rim], "space", -GH)
    front_rim = jnp.where(depth_tile > 0, front_rim, jnp.zeros_like(front_rim))
    back_rim = jnp.where(depth_tile < grid_depth - 1, back_rim, jnp.zeros_like(back_rim))
    return jnp.concatenate([front_rim, taller, back_rim], 0)


def width_taps(acc, out_count):
    width = acc.shape[1]
    col = lax.broadcasted_iota(jnp.int32, (out_count, width), 1)
    left = pltpu.roll(acc[:out_count], 1, 1)
    right = pltpu.roll(acc[2 * out_count :], width - 1, 1)
    left = jnp.where(col > 0, left, 0.0)
    right = jnp.where(col < width - 1, right, 0.0)
    return left + acc[out_count : 2 * out_count] + right


def conv_rows(src_ref, w_ref, d, h, out_count):
    windows = []
    for a in range(3):
        window = src_ref[d + a, pl.ds(h, 3)]
        windows.append(window.reshape(-1, window.shape[-1]))
    acc = jnp.dot(w_ref[...], jnp.concatenate(windows, 0), preferred_element_type=jnp.float32)
    return width_taps(acc, out_count)


def two_layers_kernel(keep_ref, x_ref, w1_ref, w2_ref, o_ref, hid_ref):
    mid_count = w1_ref.shape[0] // 3
    out_count = w2_ref.shape[0] // 3
    hid_depth, hid_height = hid_ref.shape[0], hid_ref.shape[1]
    out_depth, out_height = o_ref.shape[0], o_ref.shape[1]

    for d in range(hid_depth):
        def first(h, carry, d=d):
            y = jnp.maximum(conv_rows(x_ref, w1_ref, d, h, mid_count), 0.0)
            y = jnp.where(keep_ref[d * hid_height + h] > 0, y, 0.0)
            hid_ref[d, h] = y.astype(hid_ref.dtype)
            return carry

        lax.fori_loop(0, hid_height, first, 0)

    for d in range(out_depth):
        def second(h, carry, d=d):
            y = jnp.maximum(conv_rows(hid_ref, w2_ref, d, h, out_count), 0.0)
            o_ref[d, h] = y.astype(o_ref.dtype)
            return carry

        lax.fori_loop(0, out_height, second, 0)


def two_layers(keep, padded, w1, w2):
    in_depth, in_height, _, width = padded.shape
    mid_count = w1.shape[0] // 3
    out_count = w2.shape[0] // 3
    vmem = pltpu.MemorySpace.VMEM
    return pl.pallas_call(
        two_layers_kernel,
        out_shape=jax.ShapeDtypeStruct((in_depth - 4, in_height - 4, out_count, width), jnp.bfloat16),
        in_specs=[
            pl.BlockSpec(memory_space=pltpu.SMEM),
            pl.BlockSpec(memory_space=vmem),
            pl.BlockSpec(memory_space=vmem),
            pl.BlockSpec(memory_space=vmem),
        ],
        out_specs=pl.BlockSpec(memory_space=vmem),
        scratch_shapes=[pltpu.VMEM((in_depth - 2, in_height - 2, mid_count, width), jnp.bfloat16)],
    )(keep, padded, w1, w2)


def tap_matrices(filters):
    a, b, e, o, c = filters.shape
    return filters.transpose(2, 3, 0, 1, 4).reshape(e * o, a * b * c)


def inside_flags(depth_rows, height_rows):
    tile_row, depth_tile, grid_depth = tile_place()
    d = lax.broadcasted_iota(jnp.int32, (depth_rows, height_rows), 0)
    h = lax.broadcasted_iota(jnp.int32, (depth_rows, height_rows), 1)
    keep = (d > 0) | (depth_tile > 0)
    keep &= (d < depth_rows - 1) | (depth_tile < grid_depth - 1)
    keep &= (h > 0) | (tile_row > 0)
    keep &= (h < height_rows - 1) | (tile_row < GH - 1)
    return keep.astype(jnp.int32).reshape(-1)


def local(voxels, first_filters, second_filters):
    all_first = lax.all_gather(first_filters, "chan", axis=3, tiled=True)
    tile = voxels.transpose(1, 2, 0, 3)
    padded = wide_border(tile, 2)
    keep = inside_flags(padded.shape[0] - 2, padded.shape[1] - 2)
    out = two_layers(keep, padded, tap_matrices(all_first), tap_matrices(second_filters))
    return out.transpose(2, 0, 1, 3)


def solution(mesh):
    return jax.shard_map(
        local,
        mesh=mesh,
        in_specs=(
            P(None, "space", None, None),
            P(None, None, None, "chan", None),
            P(None, None, None, "chan", None),
        ),
        out_specs=P("chan", "space", None, None),
        check_vma=False,
    )
```

```python
import functools

import jax
import jax.numpy as jnp
from jax import lax
from jax.experimental import pallas as pl
from jax.experimental.pallas import tpu as pltpu
from jax.sharding import PartitionSpec as P

GH = 8


def passed_along(value, axis, steps):
    count = lax.axis_size(axis)
    pairs = [(source, (source + steps) % count) for source in range(count)]
    return lax.ppermute(value, axis, pairs)


def tile_place():
    tile_count = lax.axis_size("space")
    position = (lax.axis_index("space") + GH + GH // 4) % tile_count
    return position % GH, position // GH, tile_count // GH


def shared_along(value, steps):
    core = lax.axis_index("chan") % 2
    half = value.shape[1] // 2
    mine = lax.dynamic_slice_in_dim(value, core * half, half, 1)
    mine = passed_along(mine, "space", steps)
    count = lax.axis_size("chan")
    theirs = lax.ppermute(mine, "chan", [(source, source ^ 1) for source in range(count)])
    return jnp.where(core == 0, jnp.concatenate([mine, theirs], 1), jnp.concatenate([theirs, mine], 1))


def wide_border(volume_tile, rim):
    tile_row, depth_tile, grid_depth = tile_place()
    above_rim = passed_along(volume_tile[:, -rim:], "space", 1)
    below_rim = passed_along(volume_tile[:, :rim], "space", -1)
    above_rim = jnp.where(tile_row > 0, above_rim, jnp.zeros_like(above_rim))
    below_rim = jnp.where(tile_row < GH - 1, below_rim, jnp.zeros_like(below_rim))
    taller = jnp.concatenate([above_rim, volume_tile, below_rim], 1)
    front_rim = shared_along(taller[-rim:], GH)
    back_rim = shared_along(taller[:rim], -GH)
    front_rim = jnp.where(depth_tile > 0, front_rim, jnp.zeros_like(front_rim))
    back_rim = jnp.where(depth_tile < grid_depth - 1, back_rim, jnp.zeros_like(back_rim))
    return jnp.concatenate([front_rim, taller, back_rim], 0)


def width_taps(acc, out_count):
    width = acc.shape[1]
    col = lax.broadcasted_iota(jnp.int32, (out_count, width), 1)
    left = pltpu.roll(acc[:out_count], 1, 1)
    right = pltpu.roll(acc[2 * out_count :], width - 1, 1)
    left = jnp.where(col > 0, left, 0.0)
    right = jnp.where(col < width - 1, right, 0.0)
    return left + acc[out_count : 2 * out_count] + right


def conv_rows(src_ref, w_ref, d, h, out_count):
    windows = []
    for a in range(3):
        window = src_ref[d + a, pl.ds(h, 3)]
        windows.append(window.reshape(-1, window.shape[-1]))
    acc = jnp.dot(w_ref[...], jnp.concatenate(windows, 0), preferred_element_type=jnp.float32)
    return width_taps(acc, out_count)


def two_layers_kernel(keep_ref, x_ref, w1_ref, w2_ref, o_ref, hid_ref):
    mid_count = w1_ref.shape[0] // 3
    out_count = w2_ref.shape[0] // 3
    hid_depth, hid_height = hid_ref.shape[0], hid_ref.shape[1]
    out_depth, out_height = o_ref.shape[0], o_ref.shape[1]

    for d in range(hid_depth):
        def first(h, carry, d=d):
            y = jnp.maximum(conv_rows(x_ref, w1_ref, d, h, mid_count), 0.0)
            y = jnp.where(keep_ref[d * hid_height + h] > 0, y, 0.0)
            hid_ref[d, h] = y.astype(hid_ref.dtype)
            return carry

        lax.fori_loop(0, hid_height, first, 0)

    for d in range(out_depth):
        def second(h, carry, d=d):
            y = jnp.maximum(conv_rows(hid_ref, w2_ref, d, h, out_count), 0.0)
            o_ref[d, h] = y.astype(o_ref.dtype)
            return carry

        lax.fori_loop(0, out_height, second, 0)


def two_layers(keep, padded, w1, w2):
    in_depth, in_height, _, width = padded.shape
    mid_count = w1.shape[0] // 3
    out_count = w2.shape[0] // 3
    vmem = pltpu.MemorySpace.VMEM
    return pl.pallas_call(
        two_layers_kernel,
        out_shape=jax.ShapeDtypeStruct((in_depth - 4, in_height - 4, out_count, width), jnp.bfloat16),
        in_specs=[
            pl.BlockSpec(memory_space=pltpu.SMEM),
            pl.BlockSpec(memory_space=vmem),
            pl.BlockSpec(memory_space=vmem),
            pl.BlockSpec(memory_space=vmem),
        ],
        out_specs=pl.BlockSpec(memory_space=vmem),
        scratch_shapes=[pltpu.VMEM((in_depth - 2, in_height - 2, mid_count, width), jnp.bfloat16)],
    )(keep, padded, w1, w2)


def tap_matrices(filters):
    a, b, e, o, c = filters.shape
    return filters.transpose(2, 3, 0, 1, 4).reshape(e * o, a * b * c)


def inside_flags(depth_rows, height_rows):
    tile_row, depth_tile, grid_depth = tile_place()
    d = lax.broadcasted_iota(jnp.int32, (depth_rows, height_rows), 0)
    h = lax.broadcasted_iota(jnp.int32, (depth_rows, height_rows), 1)
    keep = (d > 0) | (depth_tile > 0)
    keep &= (d < depth_rows - 1) | (depth_tile < grid_depth - 1)
    keep &= (h > 0) | (tile_row > 0)
    keep &= (h < height_rows - 1) | (tile_row < GH - 1)
    return keep.astype(jnp.int32).reshape(-1)


def local(voxels, first_filters, second_filters):
    all_first = lax.all_gather(first_filters, "chan", axis=3, tiled=True)
    tile = voxels.transpose(1, 2, 0, 3)
    padded = wide_border(tile, 2)
    keep = inside_flags(padded.shape[0] - 2, padded.shape[1] - 2)
    out = two_layers(keep, padded, tap_matrices(all_first), tap_matrices(second_filters))
    return out.transpose(2, 0, 1, 3)


def solution(mesh):
    return jax.shard_map(
        local,
        mesh=mesh,
        in_specs=(
            P(None, "space", None, None),
            P(None, None, None, "chan", None),
            P(None, None, None, "chan", None),
        ),
        out_specs=P("chan", "space", None, None),
        check_vma=False,
    )
```

```python
import functools

import jax
import jax.numpy as jnp
from jax import lax
from jax.experimental import pallas as pl
from jax.experimental.pallas import tpu as pltpu
from jax.sharding import PartitionSpec as P

GH = 8


def passed_along(value, axis, steps):
    count = lax.axis_size(axis)
    pairs = [(source, (source + steps) % count) for source in range(count)]
    return lax.ppermute(value, axis, pairs)


def tile_place():
    tile_count = lax.axis_size("space")
    position = (lax.axis_index("space") + GH + GH // 4) % tile_count
    return position % GH, position // GH, tile_count // GH


def shared_along(value, steps):
    core = lax.axis_index("chan") % 2
    half = value.shape[1] // 2
    mine = lax.dynamic_slice_in_dim(value, core * half, half, 1)
    mine = passed_along(mine, "space", steps)
    count = lax.axis_size("chan")
    theirs = lax.ppermute(mine, "chan", [(source, source ^ 1) for source in range(count)])
    return jnp.where(core == 0, jnp.concatenate([mine, theirs], 1), jnp.concatenate([theirs, mine], 1))


def wide_border(volume_tile, rim):
    tile_row, depth_tile, grid_depth = tile_place()
    above_rim = passed_along(volume_tile[:, -rim:], "space", 1)
    below_rim = passed_along(volume_tile[:, :rim], "space", -1)
    above_rim = jnp.where(tile_row > 0, above_rim, jnp.zeros_like(above_rim))
    below_rim = jnp.where(tile_row < GH - 1, below_rim, jnp.zeros_like(below_rim))
    taller = jnp.concatenate([above_rim, volume_tile, below_rim], 1)
    front_rim = shared_along(taller[-rim:], GH)
    back_rim = shared_along(taller[:rim], -GH)
    front_rim = jnp.where(depth_tile > 0, front_rim, jnp.zeros_like(front_rim))
    back_rim = jnp.where(depth_tile < grid_depth - 1, back_rim, jnp.zeros_like(back_rim))
    return jnp.concatenate([front_rim, taller, back_rim], 0)


def width_taps(acc, out_count):
    width = acc.shape[1]
    col = lax.broadcasted_iota(jnp.int32, (out_count, width), 1)
    left = pltpu.roll(acc[:out_count], 1, 1)
    right = pltpu.roll(acc[2 * out_count :], width - 1, 1)
    left = jnp.where(col > 0, left, 0.0)
    right = jnp.where(col < width - 1, right, 0.0)
    return left + acc[out_count : 2 * out_count] + right


def conv_rows(src_ref, w_ref, d, h, out_count):
    windows = []
    for a in range(3):
        window = src_ref[d + a, pl.ds(h, 3)]
        windows.append(window.reshape(-1, window.shape[-1]))
    acc = jnp.dot(w_ref[...], jnp.concatenate(windows, 0), preferred_element_type=jnp.float32)
    return width_taps(acc, out_count)


def two_layers_kernel(keep_ref, x_ref, w1_ref, w2_ref, o_ref, hid_ref):
    mid_count = w1_ref.shape[0] // 3
    out_count = w2_ref.shape[0] // 3
    hid_depth, hid_height = hid_ref.shape[0], hid_ref.shape[1]
    out_depth, out_height = o_ref.shape[0], o_ref.shape[1]

    for d in range(hid_depth):
        def first(h, carry, d=d):
            y = jnp.maximum(conv_rows(x_ref, w1_ref, d, h, mid_count), 0.0)
            y = jnp.where(keep_ref[d * hid_height + h] > 0, y, 0.0)
            hid_ref[d, h] = y.astype(hid_ref.dtype)
            return carry

        lax.fori_loop(0, hid_height, first, 0)

    for d in range(out_depth):
        def second(h, carry, d=d):
            y = jnp.maximum(conv_rows(hid_ref, w2_ref, d, h, out_count), 0.0)
            o_ref[d, h] = y.astype(o_ref.dtype)
            return carry

        lax.fori_loop(0, out_height, second, 0)


def two_layers(keep, padded, w1, w2):
    in_depth, in_height, _, width = padded.shape
    mid_count = w1.shape[0] // 3
    out_count = w2.shape[0] // 3
    vmem = pltpu.MemorySpace.VMEM
    return pl.pallas_call(
        two_layers_kernel,
        out_shape=jax.ShapeDtypeStruct((in_depth - 4, in_height - 4, out_count, width), jnp.bfloat16),
        in_specs=[
            pl.BlockSpec(memory_space=pltpu.SMEM),
            pl.BlockSpec(memory_space=vmem),
            pl.BlockSpec(memory_space=vmem),
            pl.BlockSpec(memory_space=vmem),
        ],
        out_specs=pl.BlockSpec(memory_space=vmem),
        scratch_shapes=[pltpu.VMEM((in_depth - 2, in_height - 2, mid_count, width), jnp.bfloat16)],
    )(keep, padded, w1, w2)


def tap_matrices(filters):
    a, b, e, o, c = filters.shape
    return filters.transpose(2, 3, 0, 1, 4).reshape(e * o, a * b * c)


def inside_flags(depth_rows, height_rows):
    tile_row, depth_tile, grid_depth = tile_place()
    d = lax.broadcasted_iota(jnp.int32, (depth_rows, height_rows), 0)
    h = lax.broadcasted_iota(jnp.int32, (depth_rows, height_rows), 1)
    keep = (d > 0) | (depth_tile > 0)
    keep &= (d < depth_rows - 1) | (depth_tile < grid_depth - 1)
    keep &= (h > 0) | (tile_row > 0)
    keep &= (h < height_rows - 1) | (tile_row < GH - 1)
    return keep.astype(jnp.int32).reshape(-1)


def gathered_filters(first_filters, second_filters):
    count = lax.axis_size("chan")
    own = lax.axis_index("chan")
    pieces = [first_filters]
    for steps in range(1, count):
        pieces.append(passed_along(first_filters, "chan", -steps))
    all_first = jnp.concatenate(pieces, 3)
    block = first_filters.shape[3]
    doubled = jnp.concatenate([second_filters, second_filters], 4)
    all_second = lax.dynamic_slice_in_dim(doubled, own * block, second_filters.shape[4], 4)
    return all_first, all_second


def local(voxels, first_filters, second_filters):
    all_first, second_filters = gathered_filters(first_filters, second_filters)
    tile = voxels.transpose(1, 2, 0, 3)
    padded = wide_border(tile, 2)
    keep = inside_flags(padded.shape[0] - 2, padded.shape[1] - 2)
    out = two_layers(keep, padded, tap_matrices(all_first), tap_matrices(second_filters))
    return out.transpose(2, 0, 1, 3)


def solution(mesh):
    return jax.shard_map(
        local,
        mesh=mesh,
        in_specs=(
            P(None, "space", None, None),
            P(None, None, None, "chan", None),
            P(None, None, None, "chan", None),
        ),
        out_specs=P("chan", "space", None, None),
        check_vma=False,
    )
```

```python
import functools

import jax
import jax.numpy as jnp
from jax import lax
from jax.experimental import pallas as pl
from jax.experimental.pallas import tpu as pltpu
from jax.sharding import PartitionSpec as P

GH = 8


def passed_along(value, axis, steps):
    count = lax.axis_size(axis)
    pairs = [(source, (source + steps) % count) for source in range(count)]
    return lax.ppermute(value, axis, pairs)


def tile_place():
    tile_count = lax.axis_size("space")
    position = (lax.axis_index("space") + GH + GH // 4) % tile_count
    return position % GH, position // GH, tile_count // GH


def shared_along(value, steps):
    core = lax.axis_index("chan") % 2
    half = value.shape[1] // 2
    mine = lax.dynamic_slice_in_dim(value, core * half, half, 1)
    mine = passed_along(mine, "space", steps)
    count = lax.axis_size("chan")
    theirs = lax.ppermute(mine, "chan", [(source, source ^ 1) for source in range(count)])
    return jnp.where(core == 0, jnp.concatenate([mine, theirs], 1), jnp.concatenate([theirs, mine], 1))


def wide_border(volume_tile, rim):
    tile_row, depth_tile, grid_depth = tile_place()
    above_rim = passed_along(volume_tile[:, -rim:], "space", 1)
    below_rim = passed_along(volume_tile[:, :rim], "space", -1)
    above_rim = jnp.where(tile_row > 0, above_rim, jnp.zeros_like(above_rim))
    below_rim = jnp.where(tile_row < GH - 1, below_rim, jnp.zeros_like(below_rim))
    taller = jnp.concatenate([above_rim, volume_tile, below_rim], 1)
    front_rim = shared_along(taller[-rim:], GH)
    back_rim = shared_along(taller[:rim], -GH)
    front_rim = jnp.where(depth_tile > 0, front_rim, jnp.zeros_like(front_rim))
    back_rim = jnp.where(depth_tile < grid_depth - 1, back_rim, jnp.zeros_like(back_rim))
    return jnp.concatenate([front_rim, taller, back_rim], 0)


def width_taps(acc, out_count):
    width = acc.shape[1]
    col = lax.broadcasted_iota(jnp.int32, (out_count, width), 1)
    left = pltpu.roll(acc[:out_count], 1, 1)
    right = pltpu.roll(acc[2 * out_count :], width - 1, 1)
    left = jnp.where(col > 0, left, 0.0)
    right = jnp.where(col < width - 1, right, 0.0)
    return left + acc[out_count : 2 * out_count] + right


def conv_rows(src_ref, w_ref, d, h, out_count):
    windows = []
    for a in range(3):
        window = src_ref[d + a, pl.ds(h, 3)]
        windows.append(window.reshape(-1, window.shape[-1]))
    acc = jnp.dot(w_ref[...], jnp.concatenate(windows, 0), preferred_element_type=jnp.float32)
    return width_taps(acc, out_count)


def two_layers_kernel(keep_ref, x_ref, w1_ref, w2_ref, o_ref, hid_ref):
    mid_count = w1_ref.shape[0] // 3
    out_count = w2_ref.shape[0] // 3
    hid_depth, hid_height = hid_ref.shape[0], hid_ref.shape[1]
    out_depth, out_height = o_ref.shape[0], o_ref.shape[1]

    for d in range(hid_depth):
        def first(h, carry, d=d):
            y = jnp.maximum(conv_rows(x_ref, w1_ref, d, h, mid_count), 0.0)
            y = jnp.where(keep_ref[d * hid_height + h] > 0, y, 0.0)
            hid_ref[d, h] = y.astype(hid_ref.dtype)
            return carry

        lax.fori_loop(0, hid_height, first, 0, unroll=True)

    for d in range(out_depth):
        def second(h, carry, d=d):
            y = jnp.maximum(conv_rows(hid_ref, w2_ref, d, h, out_count), 0.0)
            o_ref[d, h] = y.astype(o_ref.dtype)
            return carry

        lax.fori_loop(0, out_height, second, 0, unroll=True)


def two_layers(keep, padded, w1, w2):
    in_depth, in_height, _, width = padded.shape
    mid_count = w1.shape[0] // 3
    out_count = w2.shape[0] // 3
    vmem = pltpu.MemorySpace.VMEM
    return pl.pallas_call(
        two_layers_kernel,
        out_shape=jax.ShapeDtypeStruct((in_depth - 4, in_height - 4, out_count, width), jnp.bfloat16),
        in_specs=[
            pl.BlockSpec(memory_space=pltpu.SMEM),
            pl.BlockSpec(memory_space=vmem),
            pl.BlockSpec(memory_space=vmem),
            pl.BlockSpec(memory_space=vmem),
        ],
        out_specs=pl.BlockSpec(memory_space=vmem),
        scratch_shapes=[pltpu.VMEM((in_depth - 2, in_height - 2, mid_count, width), jnp.bfloat16)],
    )(keep, padded, w1, w2)


def tap_matrices(filters):
    a, b, e, o, c = filters.shape
    return filters.transpose(2, 3, 0, 1, 4).reshape(e * o, a * b * c)


def inside_flags(depth_rows, height_rows):
    tile_row, depth_tile, grid_depth = tile_place()
    d = lax.broadcasted_iota(jnp.int32, (depth_rows, height_rows), 0)
    h = lax.broadcasted_iota(jnp.int32, (depth_rows, height_rows), 1)
    keep = (d > 0) | (depth_tile > 0)
    keep &= (d < depth_rows - 1) | (depth_tile < grid_depth - 1)
    keep &= (h > 0) | (tile_row > 0)
    keep &= (h < height_rows - 1) | (tile_row < GH - 1)
    return keep.astype(jnp.int32).reshape(-1)


def gathered_filters(first_filters, second_filters):
    count = lax.axis_size("chan")
    own = lax.axis_index("chan")
    pieces = [first_filters]
    for steps in range(1, count):
        pieces.append(passed_along(first_filters, "chan", -steps))
    all_first = jnp.concatenate(pieces, 3)
    block = first_filters.shape[3]
    doubled = jnp.concatenate([second_filters, second_filters], 4)
    all_second = lax.dynamic_slice_in_dim(doubled, own * block, second_filters.shape[4], 4)
    return all_first, all_second


def local(voxels, first_filters, second_filters):
    all_first, second_filters = gathered_filters(first_filters, second_filters)
    tile = voxels.transpose(1, 2, 0, 3)
    padded = wide_border(tile, 2)
    keep = inside_flags(padded.shape[0] - 2, padded.shape[1] - 2)
    out = two_layers(keep, padded, tap_matrices(all_first), tap_matrices(second_filters))
    return out.transpose(2, 0, 1, 3)


def solution(mesh):
    return jax.shard_map(
        local,
        mesh=mesh,
        in_specs=(
            P(None, "space", None, None),
            P(None, None, None, "chan", None),
            P(None, None, None, "chan", None),
        ),
        out_specs=P("chan", "space", None, None),
        check_vma=False,
    )
```

```python
import functools

import jax
import jax.numpy as jnp
from jax import lax
from jax.experimental import pallas as pl
from jax.experimental.pallas import tpu as pltpu
from jax.sharding import PartitionSpec as P

GH = 8


def passed_along(value, axis, steps):
    count = lax.axis_size(axis)
    pairs = [(source, (source + steps) % count) for source in range(count)]
    return lax.ppermute(value, axis, pairs)


def tile_place():
    tile_count = lax.axis_size("space")
    position = (lax.axis_index("space") + GH + GH // 4) % tile_count
    return position % GH, position // GH, tile_count // GH


def shared_along(value, steps):
    core = lax.axis_index("chan") % 2
    half = value.shape[1] // 2
    mine = lax.dynamic_slice_in_dim(value, core * half, half, 1)
    mine = passed_along(mine, "space", steps)
    count = lax.axis_size("chan")
    theirs = lax.ppermute(mine, "chan", [(source, source ^ 1) for source in range(count)])
    return jnp.where(core == 0, jnp.concatenate([mine, theirs], 1), jnp.concatenate([theirs, mine], 1))


def wide_border(volume_tile, rim):
    tile_row, depth_tile, grid_depth = tile_place()
    top = volume_tile[:, -rim:]
    bottom = volume_tile[:, :rim]
    has_above = tile_row > 0
    has_below = tile_row < GH - 1
    has_front = depth_tile > 0
    has_back = depth_tile < grid_depth - 1

    def kept(value, flag):
        return jnp.where(flag, value, jnp.zeros_like(value))

    above = kept(passed_along(top, "space", 1), has_above)
    below = kept(passed_along(bottom, "space", -1), has_below)
    front = kept(shared_along(volume_tile, GH), has_front)
    back = kept(shared_along(volume_tile, -GH), has_back)
    front_above = kept(passed_along(top, "space", GH + 1), has_front & has_above)
    front_below = kept(passed_along(bottom, "space", GH - 1), has_front & has_below)
    back_above = kept(passed_along(top, "space", 1 - GH), has_back & has_above)
    back_below = kept(passed_along(bottom, "space", -1 - GH), has_back & has_below)
    front = jnp.concatenate([front_above, front, front_below], 1)
    taller = jnp.concatenate([above, volume_tile, below], 1)
    back = jnp.concatenate([back_above, back, back_below], 1)
    return jnp.concatenate([front, taller, back], 0)


def width_taps(acc, out_count):
    width = acc.shape[1]
    col = lax.broadcasted_iota(jnp.int32, (out_count, width), 1)
    left = pltpu.roll(acc[:out_count], 1, 1)
    right = pltpu.roll(acc[2 * out_count :], width - 1, 1)
    left = jnp.where(col > 0, left, 0.0)
    right = jnp.where(col < width - 1, right, 0.0)
    return left + acc[out_count : 2 * out_count] + right


def conv_rows(src_ref, w_ref, d, h, out_count):
    windows = []
    for a in range(3):
        window = src_ref[d + a, pl.ds(h, 3)]
        windows.append(window.reshape(-1, window.shape[-1]))
    acc = jnp.dot(w_ref[...], jnp.concatenate(windows, 0), preferred_element_type=jnp.float32)
    return width_taps(acc, out_count)


def two_layers_kernel(keep_ref, x_ref, w1_ref, w2_ref, o_ref, hid_ref):
    mid_count = w1_ref.shape[0] // 3
    out_count = w2_ref.shape[0] // 3
    hid_depth, hid_height = hid_ref.shape[0], hid_ref.shape[1]
    out_depth, out_height = o_ref.shape[0], o_ref.shape[1]

    for d in range(hid_depth):
        def first(h, carry, d=d):
            y = jnp.maximum(conv_rows(x_ref, w1_ref, d, h, mid_count), 0.0)
            y = jnp.where(keep_ref[d * hid_height + h] > 0, y, 0.0)
            hid_ref[d, h] = y.astype(hid_ref.dtype)
            return carry

        lax.fori_loop(0, hid_height, first, 0, unroll=True)

    for d in range(out_depth):
        def second(h, carry, d=d):
            y = jnp.maximum(conv_rows(hid_ref, w2_ref, d, h, out_count), 0.0)
            o_ref[d, h] = y.astype(o_ref.dtype)
            return carry

        lax.fori_loop(0, out_height, second, 0, unroll=True)


def two_layers(keep, padded, w1, w2):
    in_depth, in_height, _, width = padded.shape
    mid_count = w1.shape[0] // 3
    out_count = w2.shape[0] // 3
    vmem = pltpu.MemorySpace.VMEM
    return pl.pallas_call(
        two_layers_kernel,
        out_shape=jax.ShapeDtypeStruct((in_depth - 4, in_height - 4, out_count, width), jnp.bfloat16),
        in_specs=[
            pl.BlockSpec(memory_space=pltpu.SMEM),
            pl.BlockSpec(memory_space=vmem),
            pl.BlockSpec(memory_space=vmem),
            pl.BlockSpec(memory_space=vmem),
        ],
        out_specs=pl.BlockSpec(memory_space=vmem),
        scratch_shapes=[pltpu.VMEM((in_depth - 2, in_height - 2, mid_count, width), jnp.bfloat16)],
    )(keep, padded, w1, w2)


def tap_matrices(filters):
    a, b, e, o, c = filters.shape
    return filters.transpose(2, 3, 0, 1, 4).reshape(e * o, a * b * c)


def inside_flags(depth_rows, height_rows):
    tile_row, depth_tile, grid_depth = tile_place()
    d = lax.broadcasted_iota(jnp.int32, (depth_rows, height_rows), 0)
    h = lax.broadcasted_iota(jnp.int32, (depth_rows, height_rows), 1)
    keep = (d > 0) | (depth_tile > 0)
    keep &= (d < depth_rows - 1) | (depth_tile < grid_depth - 1)
    keep &= (h > 0) | (tile_row > 0)
    keep &= (h < height_rows - 1) | (tile_row < GH - 1)
    return keep.astype(jnp.int32).reshape(-1)


def gathered_filters(first_filters, second_filters):
    count = lax.axis_size("chan")
    own = lax.axis_index("chan")
    pieces = [first_filters]
    for steps in range(1, count):
        pieces.append(passed_along(first_filters, "chan", -steps))
    all_first = jnp.concatenate(pieces, 3)
    block = first_filters.shape[3]
    doubled = jnp.concatenate([second_filters, second_filters], 4)
    all_second = lax.dynamic_slice_in_dim(doubled, own * block, second_filters.shape[4], 4)
    return all_first, all_second


def local(voxels, first_filters, second_filters):
    all_first, second_filters = gathered_filters(first_filters, second_filters)
    tile = voxels.transpose(1, 2, 0, 3)
    padded = wide_border(tile, 2)
    keep = inside_flags(padded.shape[0] - 2, padded.shape[1] - 2)
    out = two_layers(keep, padded, tap_matrices(all_first), tap_matrices(second_filters))
    return out.transpose(2, 0, 1, 3)


def solution(mesh):
    return jax.shard_map(
        local,
        mesh=mesh,
        in_specs=(
            P(None, "space", None, None),
            P(None, None, None, "chan", None),
            P(None, None, None, "chan", None),
        ),
        out_specs=P("chan", "space", None, None),
        check_vma=False,
    )
```

```python
import jax
import jax.numpy as jnp
from jax import lax
from jax.experimental import pallas as pl
from jax.experimental.pallas import tpu as pltpu
from jax.sharding import PartitionSpec as P


GH = 8


def passed_along(value, axis, steps):
    count = lax.axis_size(axis)
    pairs = [(source, (source + steps) % count) for source in range(count)]
    return lax.ppermute(value, axis, pairs)


def tile_place():
    tile_count = lax.axis_size("space")
    position = (lax.axis_index("space") + GH + GH // 4) % tile_count
    return position % GH, position // GH, tile_count // GH


def shared_along(value, steps):
    core = lax.axis_index("chan") % 2
    half = value.shape[1] // 2
    mine = lax.dynamic_slice_in_dim(value, core * half, half, 1)
    mine = passed_along(mine, "space", steps)
    count = lax.axis_size("chan")
    theirs = lax.ppermute(mine, "chan", [(source, source ^ 1) for source in range(count)])
    return jnp.where(core == 0, jnp.concatenate([mine, theirs], 1), jnp.concatenate([theirs, mine], 1))


def wide_border(volume_tile, rim):
    tile_row, depth_tile, grid_depth = tile_place()

    def kept(value, flag):
        return jnp.where(flag, value, jnp.zeros_like(value))

    above = kept(passed_along(volume_tile[:, -rim:], "space", 1), tile_row > 0)
    below = kept(passed_along(volume_tile[:, :rim], "space", -1), tile_row < GH - 1)
    taller = jnp.concatenate([above, volume_tile, below], 1)
    front = kept(shared_along(taller, GH), depth_tile > 0)
    back = kept(shared_along(taller, -GH), depth_tile < grid_depth - 1)
    return jnp.concatenate([front, taller, back], 0)


def width_taps(acc, out_count):
    width = acc.shape[1]
    col = lax.broadcasted_iota(jnp.int32, (out_count, width), 1)
    left = pltpu.roll(acc[:out_count], 1, 1)
    right = pltpu.roll(acc[2 * out_count :], width - 1, 1)
    left = jnp.where(col > 0, left, 0.0)
    right = jnp.where(col < width - 1, right, 0.0)
    return left + acc[out_count : 2 * out_count] + right


def conv_rows(src_ref, w_ref, d, h, out_count):
    windows = []
    for a in range(3):
        window = src_ref[d + a, pl.ds(h, 3)]
        windows.append(window.reshape(-1, window.shape[-1]))
    acc = jnp.dot(w_ref[...], jnp.concatenate(windows, 0), preferred_element_type=jnp.float32)
    return width_taps(acc, out_count)


def two_layers_kernel(keep_ref, x_ref, w1_ref, w2_ref, o_ref, hid_ref):
    mid_count = w1_ref.shape[0] // 3
    out_count = w2_ref.shape[0] // 3
    hid_depth, hid_height = hid_ref.shape[0], hid_ref.shape[1]
    out_depth, out_height = o_ref.shape[0], o_ref.shape[1]

    for d in range(hid_depth):
        def first(h, carry, d=d):
            y = jnp.maximum(conv_rows(x_ref, w1_ref, d, h, mid_count), 0.0)
            y = jnp.where(keep_ref[d * hid_height + h] > 0, y, 0.0)
            hid_ref[d, h] = y.astype(hid_ref.dtype)
            return carry

        lax.fori_loop(0, hid_height, first, 0, unroll=True)

    for d in range(out_depth):
        def second(h, carry, d=d):
            y = jnp.maximum(conv_rows(hid_ref, w2_ref, d, h, out_count), 0.0)
            o_ref[d, h] = y.astype(o_ref.dtype)
            return carry

        lax.fori_loop(0, out_height, second, 0, unroll=True)


def two_layers(keep, padded, w1, w2):
    in_depth, in_height, _, width = padded.shape
    mid_count = w1.shape[0] // 3
    out_count = w2.shape[0] // 3
    vmem = pltpu.MemorySpace.VMEM
    return pl.pallas_call(
        two_layers_kernel,
        out_shape=jax.ShapeDtypeStruct((in_depth - 4, in_height - 4, out_count, width), jnp.bfloat16),
        in_specs=[
            pl.BlockSpec(memory_space=pltpu.SMEM),
            pl.BlockSpec(memory_space=vmem),
            pl.BlockSpec(memory_space=vmem),
            pl.BlockSpec(memory_space=vmem),
        ],
        out_specs=pl.BlockSpec(memory_space=vmem),
        scratch_shapes=[pltpu.VMEM((in_depth - 2, in_height - 2, mid_count, width), jnp.bfloat16)],
    )(keep, padded, w1, w2)


def tap_matrices(filters):
    a, b, e, o, c = filters.shape
    return filters.transpose(2, 3, 0, 1, 4).reshape(e * o, a * b * c)


def inside_flags(depth_rows, height_rows):
    tile_row, depth_tile, grid_depth = tile_place()
    d = lax.broadcasted_iota(jnp.int32, (depth_rows, height_rows), 0)
    h = lax.broadcasted_iota(jnp.int32, (depth_rows, height_rows), 1)
    keep = (d > 0) | (depth_tile > 0)
    keep &= (d < depth_rows - 1) | (depth_tile < grid_depth - 1)
    keep &= (h > 0) | (tile_row > 0)
    keep &= (h < height_rows - 1) | (tile_row < GH - 1)
    return keep.astype(jnp.int32).reshape(-1)


def gathered_filters(first_filters, second_filters):
    count = lax.axis_size("chan")
    own = lax.axis_index("chan")
    pieces = [first_filters]
    for steps in range(1, count):
        pieces.append(passed_along(first_filters, "chan", -steps))
    all_first = jnp.concatenate(pieces, 3)
    block = first_filters.shape[3]
    doubled = jnp.concatenate([second_filters, second_filters], 4)
    all_second = lax.dynamic_slice_in_dim(doubled, own * block, second_filters.shape[4], 4)
    return all_first, all_second


def local(voxels, first_filters, second_filters):
    tile = voxels.transpose(1, 2, 0, 3)
    padded = wide_border(tile, 2)
    all_first, second_filters = gathered_filters(first_filters, second_filters)
    keep = inside_flags(padded.shape[0] - 2, padded.shape[1] - 2)
    out = two_layers(keep, padded, tap_matrices(all_first), tap_matrices(second_filters))
    return out.transpose(2, 0, 1, 3)


def solution(mesh):
    return jax.shard_map(
        local,
        mesh=mesh,
        in_specs=(
            P(None, "space", None, None),
            P(None, None, None, "chan", None),
            P(None, None, None, "chan", None),
        ),
        out_specs=P("chan", "space", None, None),
        check_vma=False,
    )
```

```python
import jax
import jax.numpy as jnp
from jax import lax
from jax.experimental import pallas as pl
from jax.experimental.pallas import tpu as pltpu
from jax.sharding import PartitionSpec as P


GH = 8


def passed_along(value, axis, steps):
    count = lax.axis_size(axis)
    pairs = [(source, (source + steps) % count) for source in range(count)]
    return lax.ppermute(value, axis, pairs)


def tile_place():
    tile_count = lax.axis_size("space")
    position = (lax.axis_index("space") + GH + GH // 4) % tile_count
    return position % GH, position // GH, tile_count // GH


def shared_along(value, steps):
    core = lax.axis_index("chan") % 2
    half = value.shape[1] // 2
    mine = lax.dynamic_slice_in_dim(value, core * half, half, 1)
    mine = passed_along(mine, "space", steps)
    count = lax.axis_size("chan")
    theirs = lax.ppermute(mine, "chan", [(source, source ^ 1) for source in range(count)])
    return mine, theirs


def halo_pieces(volume_tile, rim):
    tile_row, depth_tile, grid_depth = tile_place()
    top = volume_tile[:, -rim:]
    bottom = volume_tile[:, :rim]
    front = shared_along(volume_tile, GH)
    back = shared_along(volume_tile, -GH)
    above = passed_along(top, "space", 1)
    below = passed_along(bottom, "space", -1)
    front_above = passed_along(top, "space", GH + 1)
    front_below = passed_along(bottom, "space", GH - 1)
    back_above = passed_along(top, "space", 1 - GH)
    back_below = passed_along(bottom, "space", -1 - GH)
    place = jnp.stack([
        tile_row > 0, tile_row < GH - 1, depth_tile > 0, depth_tile < grid_depth - 1,
    ]).astype(jnp.int32)
    place = jnp.concatenate([place, (lax.axis_index("chan") % 2).astype(jnp.int32)[None]])
    pieces = (volume_tile, above, below) + front + back + (front_above, front_below, back_above, back_below)
    return place, pieces


def width_taps(acc, out_count):
    width = acc.shape[1]
    col = lax.broadcasted_iota(jnp.int32, (out_count, width), 1)
    left = pltpu.roll(acc[:out_count], 1, 1)
    right = pltpu.roll(acc[2 * out_count :], width - 1, 1)
    left = jnp.where(col > 0, left, 0.0)
    right = jnp.where(col < width - 1, right, 0.0)
    return left + acc[out_count : 2 * out_count] + right


def conv_rows(src_ref, w_ref, d, h, out_count):
    windows = []
    for a in range(3):
        window = src_ref[d + a, pl.ds(h, 3)]
        windows.append(window.reshape(-1, window.shape[-1]))
    acc = jnp.dot(w_ref[...], jnp.concatenate(windows, 0), preferred_element_type=jnp.float32)
    return width_taps(acc, out_count)


def assemble(place_ref, own_ref, above_ref, below_ref, front_refs, back_refs, corner_refs, x_ref):
    has_above, has_below = place_ref[0] > 0, place_ref[1] > 0
    has_front, has_back = place_ref[2] > 0, place_ref[3] > 0
    core = place_ref[4]
    depth, height = own_ref.shape[0], own_ref.shape[1]
    half = height // 2

    def put(rows, cols, value, flag):
        x_ref[rows, cols] = jnp.where(flag, value, jnp.zeros_like(value))

    put(slice(2, 2 + depth), slice(2, 2 + height), own_ref[...], True)
    put(slice(2, 2 + depth), slice(0, 2), above_ref[...], has_above)
    put(slice(2, 2 + depth), slice(2 + height, 4 + height), below_ref[...], has_below)
    for (mine_ref, theirs_ref), rows, flag in (
        (front_refs, slice(0, 2), has_front),
        (back_refs, slice(2 + depth, 4 + depth), has_back),
    ):
        put(rows, pl.ds(2 + core * half, half), mine_ref[...], flag)
        put(rows, pl.ds(2 + (1 - core) * half, half), theirs_ref[...], flag)
    fa_ref, fb_ref, ba_ref, bb_ref = corner_refs
    put(slice(0, 2), slice(0, 2), fa_ref[...], has_front & has_above)
    put(slice(0, 2), slice(2 + height, 4 + height), fb_ref[...], has_front & has_below)
    put(slice(2 + depth, 4 + depth), slice(0, 2), ba_ref[...], has_back & has_above)
    put(slice(2 + depth, 4 + depth), slice(2 + height, 4 + height), bb_ref[...], has_back & has_below)


def two_layers_kernel(keep_ref, place_ref, own_ref, above_ref, below_ref, fm_ref, ft_ref, bm_ref, bt_ref,
                      fa_ref, fb_ref, ba_ref, bb_ref, w1_ref, w2_ref, o_ref, x_ref, hid_ref):
    assemble(place_ref, own_ref, above_ref, below_ref, (fm_ref, ft_ref), (bm_ref, bt_ref),
             (fa_ref, fb_ref, ba_ref, bb_ref), x_ref)
    mid_count = w1_ref.shape[0] // 3
    out_count = w2_ref.shape[0] // 3
    hid_depth, hid_height = hid_ref.shape[0], hid_ref.shape[1]
    out_depth, out_height = o_ref.shape[0], o_ref.shape[1]

    for d in range(hid_depth):
        def first(h, carry, d=d):
            y = jnp.maximum(conv_rows(x_ref, w1_ref, d, h, mid_count), 0.0)
            y = jnp.where(keep_ref[d * hid_height + h] > 0, y, 0.0)
            hid_ref[d, h] = y.astype(hid_ref.dtype)
            return carry

        lax.fori_loop(0, hid_height, first, 0, unroll=True)

    for d in range(out_depth):
        def second(h, carry, d=d):
            y = jnp.maximum(conv_rows(hid_ref, w2_ref, d, h, out_count), 0.0)
            o_ref[d, h] = y.astype(o_ref.dtype)
            return carry

        lax.fori_loop(0, out_height, second, 0, unroll=True)


def two_layers(keep, place, pieces, w1, w2):
    own = pieces[0]
    depth, height, in_count, width = own.shape
    mid_count = w1.shape[0] // 3
    out_count = w2.shape[0] // 3
    vmem = pltpu.MemorySpace.VMEM
    smem = pl.BlockSpec(memory_space=pltpu.SMEM)
    return pl.pallas_call(
        two_layers_kernel,
        out_shape=jax.ShapeDtypeStruct((depth, height, out_count, width), jnp.bfloat16),
        in_specs=[smem, smem] + [pl.BlockSpec(memory_space=vmem)] * (len(pieces) + 2),
        out_specs=pl.BlockSpec(memory_space=vmem),
        scratch_shapes=[
            pltpu.VMEM((depth + 4, height + 4, in_count, width), jnp.bfloat16),
            pltpu.VMEM((depth + 2, height + 2, mid_count, width), jnp.bfloat16),
        ],
    )(keep, place, *pieces, w1, w2)


def tap_matrices(filters):
    a, b, e, o, c = filters.shape
    return filters.transpose(2, 3, 0, 1, 4).reshape(e * o, a * b * c)


def inside_flags(depth_rows, height_rows):
    tile_row, depth_tile, grid_depth = tile_place()
    d = lax.broadcasted_iota(jnp.int32, (depth_rows, height_rows), 0)
    h = lax.broadcasted_iota(jnp.int32, (depth_rows, height_rows), 1)
    keep = (d > 0) | (depth_tile > 0)
    keep &= (d < depth_rows - 1) | (depth_tile < grid_depth - 1)
    keep &= (h > 0) | (tile_row > 0)
    keep &= (h < height_rows - 1) | (tile_row < GH - 1)
    return keep.astype(jnp.int32).reshape(-1)


def gathered_filters(first_filters, second_filters):
    count = lax.axis_size("chan")
    own = lax.axis_index("chan")
    a, b, e, block, c = first_filters.shape
    own_block = first_filters.transpose(2, 3, 0, 1, 4).reshape(e, block, a * b * c)
    pieces = [own_block]
    for steps in range(1, count):
        pieces.append(passed_along(own_block, "chan", -steps))
    all_first = jnp.concatenate(pieces, 1).reshape(e * block * count, a * b * c)
    doubled = jnp.concatenate([second_filters, second_filters], 4)
    all_second = lax.dynamic_slice_in_dim(doubled, own * block, second_filters.shape[4], 4)
    return all_first, all_second


def local(voxels, first_filters, second_filters):
    tile = voxels.transpose(1, 2, 0, 3)
    place, pieces = halo_pieces(tile, 2)
    all_first, second_filters = gathered_filters(first_filters, second_filters)
    keep = inside_flags(tile.shape[0] + 2, tile.shape[1] + 2)
    out = two_layers(keep, place, pieces, all_first, tap_matrices(second_filters))
    return out.transpose(2, 0, 1, 3)


def solution(mesh):
    return jax.shard_map(
        local,
        mesh=mesh,
        in_specs=(
            P(None, "space", None, None),
            P(None, None, None, "chan", None),
            P(None, None, None, "chan", None),
        ),
        out_specs=P("chan", "space", None, None),
        check_vma=False,
    )
```

```python
import jax
import jax.numpy as jnp
from jax import lax
from jax.experimental import pallas as pl
from jax.experimental.pallas import tpu as pltpu
from jax.sharding import PartitionSpec as P


GH = 8


def passed_along(value, axis, steps):
    count = lax.axis_size(axis)
    pairs = [(source, (source + steps) % count) for source in range(count)]
    return lax.ppermute(value, axis, pairs)


def tile_place():
    tile_count = lax.axis_size("space")
    position = (lax.axis_index("space") + GH + GH // 4) % tile_count
    return position % GH, position // GH, tile_count // GH


def shared_along(mine, steps):
    mine = passed_along(mine, "space", steps)
    count = lax.axis_size("chan")
    theirs = lax.ppermute(mine, "chan", [(source, source ^ 1) for source in range(count)])
    return mine, theirs


def halo_pieces(voxels, rim):
    tile_row, depth_tile, grid_depth = tile_place()
    core = lax.axis_index("chan") % 2
    half = voxels.shape[2] // 2
    mine = lax.dynamic_slice_in_dim(voxels, core * half, half, 2).transpose(1, 2, 0, 3)
    front = shared_along(mine, GH)
    back = shared_along(mine, -GH)
    volume_tile = voxels.transpose(1, 2, 0, 3)
    top = volume_tile[:, -rim:]
    bottom = volume_tile[:, :rim]
    above = passed_along(top, "space", 1)
    below = passed_along(bottom, "space", -1)
    front_above = passed_along(top, "space", GH + 1)
    front_below = passed_along(bottom, "space", GH - 1)
    back_above = passed_along(top, "space", 1 - GH)
    back_below = passed_along(bottom, "space", -1 - GH)
    place = jnp.stack([
        tile_row > 0, tile_row < GH - 1, depth_tile > 0, depth_tile < grid_depth - 1,
    ]).astype(jnp.int32)
    place = jnp.concatenate([place, (lax.axis_index("chan") % 2).astype(jnp.int32)[None]])
    pieces = (volume_tile, above, below) + front + back + (front_above, front_below, back_above, back_below)
    return place, pieces


def width_taps(acc, out_count):
    width = acc.shape[1]
    col = lax.broadcasted_iota(jnp.int32, (out_count, width), 1)
    left = pltpu.roll(acc[:out_count], 1, 1)
    right = pltpu.roll(acc[2 * out_count :], width - 1, 1)
    left = jnp.where(col > 0, left, 0.0)
    right = jnp.where(col < width - 1, right, 0.0)
    return left + acc[out_count : 2 * out_count] + right


def conv_rows(src_ref, w_ref, d, h, out_count):
    windows = []
    for a in range(3):
        window = src_ref[d + a, pl.ds(h, 3)]
        windows.append(window.reshape(-1, window.shape[-1]))
    acc = jnp.dot(w_ref[...], jnp.concatenate(windows, 0), preferred_element_type=jnp.float32)
    return width_taps(acc, out_count)


def assemble(place_ref, own_ref, above_ref, below_ref, front_refs, back_refs, corner_refs, x_ref):
    has_above, has_below = place_ref[0] > 0, place_ref[1] > 0
    has_front, has_back = place_ref[2] > 0, place_ref[3] > 0
    core = place_ref[4]
    depth, height = own_ref.shape[0], own_ref.shape[1]
    half = height // 2

    def put(rows, cols, value, flag):
        x_ref[rows, cols] = jnp.where(flag, value, jnp.zeros_like(value))

    put(slice(2, 2 + depth), slice(2, 2 + height), own_ref[...], True)
    put(slice(2, 2 + depth), slice(0, 2), above_ref[...], has_above)
    put(slice(2, 2 + depth), slice(2 + height, 4 + height), below_ref[...], has_below)
    for (mine_ref, theirs_ref), rows, flag in (
        (front_refs, slice(0, 2), has_front),
        (back_refs, slice(2 + depth, 4 + depth), has_back),
    ):
        put(rows, pl.ds(2 + core * half, half), mine_ref[...], flag)
        put(rows, pl.ds(2 + (1 - core) * half, half), theirs_ref[...], flag)
    fa_ref, fb_ref, ba_ref, bb_ref = corner_refs
    put(slice(0, 2), slice(0, 2), fa_ref[...], has_front & has_above)
    put(slice(0, 2), slice(2 + height, 4 + height), fb_ref[...], has_front & has_below)
    put(slice(2 + depth, 4 + depth), slice(0, 2), ba_ref[...], has_back & has_above)
    put(slice(2 + depth, 4 + depth), slice(2 + height, 4 + height), bb_ref[...], has_back & has_below)


def two_layers_kernel(keep_ref, place_ref, own_ref, above_ref, below_ref, fm_ref, ft_ref, bm_ref, bt_ref,
                      fa_ref, fb_ref, ba_ref, bb_ref, w1_ref, w2_ref, o_ref, x_ref, hid_ref):
    assemble(place_ref, own_ref, above_ref, below_ref, (fm_ref, ft_ref), (bm_ref, bt_ref),
             (fa_ref, fb_ref, ba_ref, bb_ref), x_ref)
    mid_count = w1_ref.shape[0] // 3
    out_count = w2_ref.shape[0] // 3
    hid_depth, hid_height = hid_ref.shape[0], hid_ref.shape[1]
    out_depth, out_height = o_ref.shape[0], o_ref.shape[1]

    for d in range(hid_depth):
        def first(h, carry, d=d):
            y = jnp.maximum(conv_rows(x_ref, w1_ref, d, h, mid_count), 0.0)
            y = jnp.where(keep_ref[d * hid_height + h] > 0, y, 0.0)
            hid_ref[d, h] = y.astype(hid_ref.dtype)
            return carry

        lax.fori_loop(0, hid_height, first, 0, unroll=True)

    for d in range(out_depth):
        def second(h, carry, d=d):
            y = jnp.maximum(conv_rows(hid_ref, w2_ref, d, h, out_count), 0.0)
            o_ref[d, h] = y.astype(o_ref.dtype)
            return carry

        lax.fori_loop(0, out_height, second, 0, unroll=True)


def two_layers(keep, place, pieces, w1, w2):
    own = pieces[0]
    depth, height, in_count, width = own.shape
    mid_count = w1.shape[0] // 3
    out_count = w2.shape[0] // 3
    vmem = pltpu.MemorySpace.VMEM
    smem = pl.BlockSpec(memory_space=pltpu.SMEM)
    return pl.pallas_call(
        two_layers_kernel,
        out_shape=jax.ShapeDtypeStruct((depth, height, out_count, width), jnp.bfloat16),
        in_specs=[smem, smem] + [pl.BlockSpec(memory_space=vmem)] * (len(pieces) + 2),
        out_specs=pl.BlockSpec(memory_space=vmem),
        scratch_shapes=[
            pltpu.VMEM((depth + 4, height + 4, in_count, width), jnp.bfloat16),
            pltpu.VMEM((depth + 2, height + 2, mid_count, width), jnp.bfloat16),
        ],
    )(keep, place, *pieces, w1, w2)


def tap_matrices(filters):
    a, b, e, o, c = filters.shape
    return filters.transpose(2, 3, 0, 1, 4).reshape(e * o, a * b * c)


def inside_flags(depth_rows, height_rows):
    tile_row, depth_tile, grid_depth = tile_place()
    d = lax.broadcasted_iota(jnp.int32, (depth_rows, height_rows), 0)
    h = lax.broadcasted_iota(jnp.int32, (depth_rows, height_rows), 1)
    keep = (d > 0) | (depth_tile > 0)
    keep &= (d < depth_rows - 1) | (depth_tile < grid_depth - 1)
    keep &= (h > 0) | (tile_row > 0)
    keep &= (h < height_rows - 1) | (tile_row < GH - 1)
    return keep.astype(jnp.int32).reshape(-1)


def gathered_filters(first_filters, second_filters):
    count = lax.axis_size("chan")
    own = lax.axis_index("chan")
    a, b, e, block, c = first_filters.shape
    own_block = first_filters.transpose(2, 3, 0, 1, 4).reshape(e, block, a * b * c)
    pieces = [own_block]
    for steps in range(1, count):
        pieces.append(passed_along(own_block, "chan", -steps))
    all_first = jnp.concatenate(pieces, 1).reshape(e * block * count, a * b * c)
    doubled = jnp.concatenate([second_filters, second_filters], 4)
    all_second = lax.dynamic_slice_in_dim(doubled, own * block, second_filters.shape[4], 4)
    return all_first, all_second


def local(voxels, first_filters, second_filters):
    place, pieces = halo_pieces(voxels, 2)
    all_first, second_filters = gathered_filters(first_filters, second_filters)
    keep = inside_flags(voxels.shape[1] + 2, voxels.shape[2] + 2)
    out = two_layers(keep, place, pieces, all_first, tap_matrices(second_filters))
    return out.transpose(2, 0, 1, 3)


def solution(mesh):
    return jax.shard_map(
        local,
        mesh=mesh,
        in_specs=(
            P(None, "space", None, None),
            P(None, None, None, "chan", None),
            P(None, None, None, "chan", None),
        ),
        out_specs=P("chan", "space", None, None),
        check_vma=False,
    )
```

```python
import jax
import jax.numpy as jnp
from jax import lax
from jax.experimental import pallas as pl
from jax.experimental.pallas import tpu as pltpu
from jax.sharding import PartitionSpec as P


GH = 8


def passed_along(value, axis, steps):
    count = lax.axis_size(axis)
    pairs = [(source, (source + steps) % count) for source in range(count)]
    return lax.ppermute(value, axis, pairs)


def tile_place():
    tile_count = lax.axis_size("space")
    position = (lax.axis_index("space") + GH + GH // 4) % tile_count
    return position % GH, position // GH, tile_count // GH


def shared_along(mine, steps):
    mine = passed_along(mine, "space", steps)
    count = lax.axis_size("chan")
    theirs = lax.ppermute(mine, "chan", [(source, source ^ 1) for source in range(count)])
    return mine, theirs


def halo_pieces(voxels, rim):
    tile_row, depth_tile, grid_depth = tile_place()
    core = lax.axis_index("chan") % 2
    half = voxels.shape[2] // 2
    mine = lax.dynamic_slice_in_dim(voxels, core * half, half, 2).transpose(1, 2, 0, 3)
    front = shared_along(mine, GH)
    back = shared_along(mine, -GH)
    volume_tile = voxels.transpose(1, 2, 0, 3)
    top = volume_tile[:, -rim:]
    bottom = volume_tile[:, :rim]
    above = passed_along(top, "space", 1)
    below = passed_along(bottom, "space", -1)
    rims = jnp.concatenate([above, below], 1)
    front_corners = passed_along(rims, "space", GH)
    back_corners = passed_along(rims, "space", -GH)
    front_above, front_below = front_corners[:, :rim], front_corners[:, rim:]
    back_above, back_below = back_corners[:, :rim], back_corners[:, rim:]
    place = jnp.stack([
        tile_row > 0, tile_row < GH - 1, depth_tile > 0, depth_tile < grid_depth - 1,
    ]).astype(jnp.int32)
    place = jnp.concatenate([place, (lax.axis_index("chan") % 2).astype(jnp.int32)[None]])
    pieces = (volume_tile, above, below) + front + back + (front_above, front_below, back_above, back_below)
    return place, pieces


def width_taps(acc, out_count):
    width = acc.shape[1]
    col = lax.broadcasted_iota(jnp.int32, (out_count, width), 1)
    left = pltpu.roll(acc[:out_count], 1, 1)
    right = pltpu.roll(acc[2 * out_count :], width - 1, 1)
    left = jnp.where(col > 0, left, 0.0)
    right = jnp.where(col < width - 1, right, 0.0)
    return left + acc[out_count : 2 * out_count] + right


def conv_rows(src_ref, w_ref, d, h, out_count):
    windows = []
    for a in range(3):
        window = src_ref[d + a, pl.ds(h, 3)]
        windows.append(window.reshape(-1, window.shape[-1]))
    acc = jnp.dot(w_ref[...], jnp.concatenate(windows, 0), preferred_element_type=jnp.float32)
    return width_taps(acc, out_count)


def assemble(place_ref, own_ref, above_ref, below_ref, front_refs, back_refs, corner_refs, x_ref):
    has_above, has_below = place_ref[0] > 0, place_ref[1] > 0
    has_front, has_back = place_ref[2] > 0, place_ref[3] > 0
    core = place_ref[4]
    depth, height = own_ref.shape[0], own_ref.shape[1]
    half = height // 2

    def put(rows, cols, value, flag):
        x_ref[rows, cols] = jnp.where(flag, value, jnp.zeros_like(value))

    put(slice(2, 2 + depth), slice(2, 2 + height), own_ref[...], True)
    put(slice(2, 2 + depth), slice(0, 2), above_ref[...], has_above)
    put(slice(2, 2 + depth), slice(2 + height, 4 + height), below_ref[...], has_below)
    for (mine_ref, theirs_ref), rows, flag in (
        (front_refs, slice(0, 2), has_front),
        (back_refs, slice(2 + depth, 4 + depth), has_back),
    ):
        put(rows, pl.ds(2 + core * half, half), mine_ref[...], flag)
        put(rows, pl.ds(2 + (1 - core) * half, half), theirs_ref[...], flag)
    fa_ref, fb_ref, ba_ref, bb_ref = corner_refs
    put(slice(0, 2), slice(0, 2), fa_ref[...], has_front & has_above)
    put(slice(0, 2), slice(2 + height, 4 + height), fb_ref[...], has_front & has_below)
    put(slice(2 + depth, 4 + depth), slice(0, 2), ba_ref[...], has_back & has_above)
    put(slice(2 + depth, 4 + depth), slice(2 + height, 4 + height), bb_ref[...], has_back & has_below)


def two_layers_kernel(keep_ref, place_ref, own_ref, above_ref, below_ref, fm_ref, ft_ref, bm_ref, bt_ref,
                      fa_ref, fb_ref, ba_ref, bb_ref, w1_ref, w2_ref, o_ref, x_ref, hid_ref):
    assemble(place_ref, own_ref, above_ref, below_ref, (fm_ref, ft_ref), (bm_ref, bt_ref),
             (fa_ref, fb_ref, ba_ref, bb_ref), x_ref)
    mid_count = w1_ref.shape[0] // 3
    out_count = w2_ref.shape[0] // 3
    hid_depth, hid_height = hid_ref.shape[0], hid_ref.shape[1]
    out_depth, out_height = o_ref.shape[0], o_ref.shape[1]

    for d in range(hid_depth):
        def first(h, carry, d=d):
            y = jnp.maximum(conv_rows(x_ref, w1_ref, d, h, mid_count), 0.0)
            y = jnp.where(keep_ref[d * hid_height + h] > 0, y, 0.0)
            hid_ref[d, h] = y.astype(hid_ref.dtype)
            return carry

        lax.fori_loop(0, hid_height, first, 0, unroll=True)

    for d in range(out_depth):
        def second(h, carry, d=d):
            y = jnp.maximum(conv_rows(hid_ref, w2_ref, d, h, out_count), 0.0)
            o_ref[d, h] = y.astype(o_ref.dtype)
            return carry

        lax.fori_loop(0, out_height, second, 0, unroll=True)


def two_layers(keep, place, pieces, w1, w2):
    own = pieces[0]
    depth, height, in_count, width = own.shape
    mid_count = w1.shape[0] // 3
    out_count = w2.shape[0] // 3
    vmem = pltpu.MemorySpace.VMEM
    smem = pl.BlockSpec(memory_space=pltpu.SMEM)
    return pl.pallas_call(
        two_layers_kernel,
        out_shape=jax.ShapeDtypeStruct((depth, height, out_count, width), jnp.bfloat16),
        in_specs=[smem, smem] + [pl.BlockSpec(memory_space=vmem)] * (len(pieces) + 2),
        out_specs=pl.BlockSpec(memory_space=vmem),
        scratch_shapes=[
            pltpu.VMEM((depth + 4, height + 4, in_count, width), jnp.bfloat16),
            pltpu.VMEM((depth + 2, height + 2, mid_count, width), jnp.bfloat16),
        ],
    )(keep, place, *pieces, w1, w2)


def tap_matrices(filters):
    a, b, e, o, c = filters.shape
    return filters.transpose(2, 3, 0, 1, 4).reshape(e * o, a * b * c)


def inside_flags(depth_rows, height_rows):
    tile_row, depth_tile, grid_depth = tile_place()
    d = lax.broadcasted_iota(jnp.int32, (depth_rows, height_rows), 0)
    h = lax.broadcasted_iota(jnp.int32, (depth_rows, height_rows), 1)
    keep = (d > 0) | (depth_tile > 0)
    keep &= (d < depth_rows - 1) | (depth_tile < grid_depth - 1)
    keep &= (h > 0) | (tile_row > 0)
    keep &= (h < height_rows - 1) | (tile_row < GH - 1)
    return keep.astype(jnp.int32).reshape(-1)


def gathered_filters(first_filters, second_filters):
    count = lax.axis_size("chan")
    own = lax.axis_index("chan")
    a, b, e, block, c = first_filters.shape
    own_block = first_filters.transpose(2, 3, 0, 1, 4).reshape(e, block, a * b * c)
    pieces = [own_block]
    for steps in range(1, count):
        pieces.append(passed_along(own_block, "chan", -steps))
    all_first = jnp.concatenate(pieces, 1).reshape(e * block * count, a * b * c)
    doubled = jnp.concatenate([second_filters, second_filters], 4)
    all_second = lax.dynamic_slice_in_dim(doubled, own * block, second_filters.shape[4], 4)
    return all_first, all_second


def local(voxels, first_filters, second_filters):
    place, pieces = halo_pieces(voxels, 2)
    all_first, second_filters = gathered_filters(first_filters, second_filters)
    keep = inside_flags(voxels.shape[1] + 2, voxels.shape[2] + 2)
    out = two_layers(keep, place, pieces, all_first, tap_matrices(second_filters))
    return out.transpose(2, 0, 1, 3)


def solution(mesh):
    return jax.shard_map(
        local,
        mesh=mesh,
        in_specs=(
            P(None, "space", None, None),
            P(None, None, None, "chan", None),
            P(None, None, None, "chan", None),
        ),
        out_specs=P("chan", "space", None, None),
        check_vma=False,
    )
```

```python
import jax
import jax.numpy as jnp
from jax import lax
from jax.experimental import pallas as pl
from jax.experimental.pallas import tpu as pltpu
from jax.sharding import PartitionSpec as P


GH = 8


def passed_along(value, axis, steps):
    count = lax.axis_size(axis)
    pairs = [(source, (source + steps) % count) for source in range(count)]
    return lax.ppermute(value, axis, pairs)


def tile_place():
    tile_count = lax.axis_size("space")
    position = (lax.axis_index("space") + GH + GH // 4) % tile_count
    return position % GH, position // GH, tile_count // GH


def shared_along(mine, steps):
    mine = passed_along(mine, "space", steps)
    count = lax.axis_size("chan")
    theirs = lax.ppermute(mine, "chan", [(source, source ^ 1) for source in range(count)])
    return mine, theirs


def halo_pieces(voxels, rim):
    tile_row, depth_tile, grid_depth = tile_place()
    core = lax.axis_index("chan") % 2
    half = voxels.shape[2] // 2
    mine = lax.dynamic_slice_in_dim(voxels, core * half, half, 2).transpose(1, 2, 0, 3)
    front = shared_along(mine, GH)
    back = shared_along(mine, -GH)
    volume_tile = voxels.transpose(1, 2, 0, 3)
    top = volume_tile[:, -rim:]
    bottom = volume_tile[:, :rim]
    above = passed_along(top, "space", 1)
    below = passed_along(bottom, "space", -1)
    front_above = passed_along(top, "space", GH + 1)
    front_below = passed_along(bottom, "space", GH - 1)
    back_above = passed_along(top, "space", 1 - GH)
    back_below = passed_along(bottom, "space", -1 - GH)
    place = jnp.stack([
        tile_row > 0, tile_row < GH - 1, depth_tile > 0, depth_tile < grid_depth - 1,
    ]).astype(jnp.int32)
    place = jnp.concatenate([place, (lax.axis_index("chan") % 2).astype(jnp.int32)[None]])
    pieces = (volume_tile, above, below) + front + back + (front_above, front_below, back_above, back_below)
    return place, pieces


def width_taps(acc, out_count):
    width = acc.shape[1]
    col = lax.broadcasted_iota(jnp.int32, (out_count, width), 1)
    left = pltpu.roll(acc[:out_count], 1, 1)
    right = pltpu.roll(acc[2 * out_count :], width - 1, 1)
    left = jnp.where(col > 0, left, 0.0)
    right = jnp.where(col < width - 1, right, 0.0)
    return left + acc[out_count : 2 * out_count] + right


def conv_rows(src_ref, w_ref, d, h, out_count):
    windows = []
    for a in range(3):
        window = src_ref[d + a, pl.ds(h, 3)]
        windows.append(window.reshape(-1, window.shape[-1]))
    acc = jnp.dot(w_ref[...], jnp.concatenate(windows, 0), preferred_element_type=jnp.float32)
    return width_taps(acc, out_count)


def assemble(place_ref, own_ref, above_ref, below_ref, front_refs, back_refs, corner_refs, x_ref):
    has_above, has_below = place_ref[0] > 0, place_ref[1] > 0
    has_front, has_back = place_ref[2] > 0, place_ref[3] > 0
    core = place_ref[4]
    depth, height = own_ref.shape[0], own_ref.shape[1]
    half = height // 2

    def put(rows, cols, value, flag):
        x_ref[rows, cols] = jnp.where(flag, value, jnp.zeros_like(value))

    put(slice(2, 2 + depth), slice(2, 2 + height), own_ref[...], True)
    put(slice(2, 2 + depth), slice(0, 2), above_ref[...], has_above)
    put(slice(2, 2 + depth), slice(2 + height, 4 + height), below_ref[...], has_below)
    for (mine_ref, theirs_ref), rows, flag in (
        (front_refs, slice(0, 2), has_front),
        (back_refs, slice(2 + depth, 4 + depth), has_back),
    ):
        put(rows, pl.ds(2 + core * half, half), mine_ref[...], flag)
        put(rows, pl.ds(2 + (1 - core) * half, half), theirs_ref[...], flag)
    fa_ref, fb_ref, ba_ref, bb_ref = corner_refs
    put(slice(0, 2), slice(0, 2), fa_ref[...], has_front & has_above)
    put(slice(0, 2), slice(2 + height, 4 + height), fb_ref[...], has_front & has_below)
    put(slice(2 + depth, 4 + depth), slice(0, 2), ba_ref[...], has_back & has_above)
    put(slice(2 + depth, 4 + depth), slice(2 + height, 4 + height), bb_ref[...], has_back & has_below)


def two_layers_kernel(keep_ref, place_ref, own_ref, above_ref, below_ref, fm_ref, ft_ref, bm_ref, bt_ref,
                      fa_ref, fb_ref, ba_ref, bb_ref, w1_ref, w2_ref, o_ref, x_ref, hid_ref):
    assemble(place_ref, own_ref, above_ref, below_ref, (fm_ref, ft_ref), (bm_ref, bt_ref),
             (fa_ref, fb_ref, ba_ref, bb_ref), x_ref)
    mid_count = w1_ref.shape[0] // 3
    out_count = w2_ref.shape[0] // 3
    hid_depth, hid_height = hid_ref.shape[0], hid_ref.shape[1]
    out_depth, out_height = o_ref.shape[1], o_ref.shape[2]

    for d in range(hid_depth):
        def first(h, carry, d=d):
            y = jnp.maximum(conv_rows(x_ref, w1_ref, d, h, mid_count), 0.0)
            y = jnp.where(keep_ref[d * hid_height + h] > 0, y, 0.0)
            hid_ref[d, h] = y.astype(hid_ref.dtype)
            return carry

        lax.fori_loop(0, hid_height, first, 0, unroll=True)

    for d in range(out_depth):
        def second(h, carry, d=d):
            y = jnp.maximum(conv_rows(hid_ref, w2_ref, d, h, out_count), 0.0)
            o_ref[:, d, h, :] = y.astype(o_ref.dtype)
            return carry

        lax.fori_loop(0, out_height, second, 0, unroll=True)


def two_layers(keep, place, pieces, w1, w2):
    own = pieces[0]
    depth, height, in_count, width = own.shape
    mid_count = w1.shape[0] // 3
    out_count = w2.shape[0] // 3
    vmem = pltpu.MemorySpace.VMEM
    smem = pl.BlockSpec(memory_space=pltpu.SMEM)
    return pl.pallas_call(
        two_layers_kernel,
        out_shape=jax.ShapeDtypeStruct((out_count, depth, height, width), jnp.bfloat16),
        in_specs=[smem, smem] + [pl.BlockSpec(memory_space=vmem)] * (len(pieces) + 2),
        out_specs=pl.BlockSpec(memory_space=vmem),
        scratch_shapes=[
            pltpu.VMEM((depth + 4, height + 4, in_count, width), jnp.bfloat16),
            pltpu.VMEM((depth + 2, height + 2, mid_count, width), jnp.bfloat16),
        ],
    )(keep, place, *pieces, w1, w2)


def tap_matrices(filters):
    a, b, e, o, c = filters.shape
    return filters.transpose(2, 3, 0, 1, 4).reshape(e * o, a * b * c)


def inside_flags(depth_rows, height_rows):
    tile_row, depth_tile, grid_depth = tile_place()
    d = lax.broadcasted_iota(jnp.int32, (depth_rows, height_rows), 0)
    h = lax.broadcasted_iota(jnp.int32, (depth_rows, height_rows), 1)
    keep = (d > 0) | (depth_tile > 0)
    keep &= (d < depth_rows - 1) | (depth_tile < grid_depth - 1)
    keep &= (h > 0) | (tile_row > 0)
    keep &= (h < height_rows - 1) | (tile_row < GH - 1)
    return keep.astype(jnp.int32).reshape(-1)


def gathered_filters(first_filters, second_filters):
    count = lax.axis_size("chan")
    own = lax.axis_index("chan")
    a, b, e, block, c = first_filters.shape
    own_block = first_filters.transpose(2, 3, 0, 1, 4).reshape(e, block, a * b * c)
    pieces = [own_block]
    for steps in range(1, count):
        pieces.append(passed_along(own_block, "chan", -steps))
    all_first = jnp.concatenate(pieces, 1).reshape(e * block * count, a * b * c)
    doubled = jnp.concatenate([second_filters, second_filters], 4)
    all_second = lax.dynamic_slice_in_dim(doubled, own * block, second_filters.shape[4], 4)
    return all_first, all_second


def local(voxels, first_filters, second_filters):
    place, pieces = halo_pieces(voxels, 2)
    all_first, second_filters = gathered_filters(first_filters, second_filters)
    keep = inside_flags(voxels.shape[1] + 2, voxels.shape[2] + 2)
    out = two_layers(keep, place, pieces, all_first, tap_matrices(second_filters))
    return out


def solution(mesh):
    return jax.shard_map(
        local,
        mesh=mesh,
        in_specs=(
            P(None, "space", None, None),
            P(None, None, None, "chan", None),
            P(None, None, None, "chan", None),
        ),
        out_specs=P("chan", "space", None, None),
        check_vma=False,
    )
```

```python
import jax
import jax.numpy as jnp
from jax import lax
from jax.experimental import pallas as pl
from jax.experimental.pallas import tpu as pltpu
from jax.sharding import PartitionSpec as P


GH = 8


def passed_along(value, axis, steps):
    count = lax.axis_size(axis)
    pairs = [(source, (source + steps) % count) for source in range(count)]
    return lax.ppermute(value, axis, pairs)


def tile_place():
    tile_count = lax.axis_size("space")
    position = (lax.axis_index("space") + GH + GH // 4) % tile_count
    return position % GH, position // GH, tile_count // GH


def shared_along(mine):
    front = passed_along(mine, "space", GH)
    back = passed_along(mine, "space", -GH)
    both = jnp.stack([front, back])
    count = lax.axis_size("chan")
    theirs = lax.ppermute(both, "chan", [(source, source ^ 1) for source in range(count)])
    return (front, theirs[0]), (back, theirs[1])


def halo_pieces(voxels, rim):
    tile_row, depth_tile, grid_depth = tile_place()
    core = lax.axis_index("chan") % 2
    half = voxels.shape[2] // 2
    mine = lax.dynamic_slice_in_dim(voxels, core * half, half, 2).transpose(1, 2, 0, 3)
    front, back = shared_along(mine)
    volume_tile = voxels.transpose(1, 2, 0, 3)
    top = volume_tile[:, -rim:]
    bottom = volume_tile[:, :rim]
    above = passed_along(top, "space", 1)
    below = passed_along(bottom, "space", -1)
    front_above = passed_along(top, "space", GH + 1)
    front_below = passed_along(bottom, "space", GH - 1)
    back_above = passed_along(top, "space", 1 - GH)
    back_below = passed_along(bottom, "space", -1 - GH)
    place = jnp.stack([
        tile_row > 0, tile_row < GH - 1, depth_tile > 0, depth_tile < grid_depth - 1,
    ]).astype(jnp.int32)
    place = jnp.concatenate([place, (lax.axis_index("chan") % 2).astype(jnp.int32)[None]])
    pieces = (volume_tile, above, below) + front + back + (front_above, front_below, back_above, back_below)
    return place, pieces


def width_taps(acc, out_count):
    width = acc.shape[1]
    col = lax.broadcasted_iota(jnp.int32, (out_count, width), 1)
    left = pltpu.roll(acc[:out_count], 1, 1)
    right = pltpu.roll(acc[2 * out_count :], width - 1, 1)
    left = jnp.where(col > 0, left, 0.0)
    right = jnp.where(col < width - 1, right, 0.0)
    return left + acc[out_count : 2 * out_count] + right


def conv_rows(src_ref, w_ref, d, h, out_count):
    windows = []
    for a in range(3):
        window = src_ref[d + a, pl.ds(h, 3)]
        windows.append(window.reshape(-1, window.shape[-1]))
    acc = jnp.dot(w_ref[...], jnp.concatenate(windows, 0), preferred_element_type=jnp.float32)
    return width_taps(acc, out_count)


def assemble(place_ref, own_ref, above_ref, below_ref, front_refs, back_refs, corner_refs, x_ref):
    has_above, has_below = place_ref[0] > 0, place_ref[1] > 0
    has_front, has_back = place_ref[2] > 0, place_ref[3] > 0
    core = place_ref[4]
    depth, height = own_ref.shape[0], own_ref.shape[1]
    half = height // 2

    def put(rows, cols, value, flag):
        x_ref[rows, cols] = jnp.where(flag, value, jnp.zeros_like(value))

    put(slice(2, 2 + depth), slice(2, 2 + height), own_ref[...], True)
    put(slice(2, 2 + depth), slice(0, 2), above_ref[...], has_above)
    put(slice(2, 2 + depth), slice(2 + height, 4 + height), below_ref[...], has_below)
    for (mine_ref, theirs_ref), rows, flag in (
        (front_refs, slice(0, 2), has_front),
        (back_refs, slice(2 + depth, 4 + depth), has_back),
    ):
        put(rows, pl.ds(2 + core * half, half), mine_ref[...], flag)
        put(rows, pl.ds(2 + (1 - core) * half, half), theirs_ref[...], flag)
    fa_ref, fb_ref, ba_ref, bb_ref = corner_refs
    put(slice(0, 2), slice(0, 2), fa_ref[...], has_front & has_above)
    put(slice(0, 2), slice(2 + height, 4 + height), fb_ref[...], has_front & has_below)
    put(slice(2 + depth, 4 + depth), slice(0, 2), ba_ref[...], has_back & has_above)
    put(slice(2 + depth, 4 + depth), slice(2 + height, 4 + height), bb_ref[...], has_back & has_below)


def two_layers_kernel(keep_ref, place_ref, own_ref, above_ref, below_ref, fm_ref, ft_ref, bm_ref, bt_ref,
                      fa_ref, fb_ref, ba_ref, bb_ref, w1_ref, w2_ref, o_ref, x_ref, hid_ref):
    assemble(place_ref, own_ref, above_ref, below_ref, (fm_ref, ft_ref), (bm_ref, bt_ref),
             (fa_ref, fb_ref, ba_ref, bb_ref), x_ref)
    mid_count = w1_ref.shape[0] // 3
    out_count = w2_ref.shape[0] // 3
    hid_depth, hid_height = hid_ref.shape[0], hid_ref.shape[1]
    out_depth, out_height = o_ref.shape[1], o_ref.shape[2]

    for d in range(hid_depth):
        def first(h, carry, d=d):
            y = jnp.maximum(conv_rows(x_ref, w1_ref, d, h, mid_count), 0.0)
            y = jnp.where(keep_ref[d * hid_height + h] > 0, y, 0.0)
            hid_ref[d, h] = y.astype(hid_ref.dtype)
            return carry

        lax.fori_loop(0, hid_height, first, 0, unroll=True)

    for d in range(out_depth):
        def second(h, carry, d=d):
            y = jnp.maximum(conv_rows(hid_ref, w2_ref, d, h, out_count), 0.0)
            o_ref[:, d, h, :] = y.astype(o_ref.dtype)
            return carry

        lax.fori_loop(0, out_height, second, 0, unroll=True)


def two_layers(keep, place, pieces, w1, w2):
    own = pieces[0]
    depth, height, in_count, width = own.shape
    mid_count = w1.shape[0] // 3
    out_count = w2.shape[0] // 3
    vmem = pltpu.MemorySpace.VMEM
    smem = pl.BlockSpec(memory_space=pltpu.SMEM)
    return pl.pallas_call(
        two_layers_kernel,
        out_shape=jax.ShapeDtypeStruct((out_count, depth, height, width), jnp.bfloat16),
        in_specs=[smem, smem] + [pl.BlockSpec(memory_space=vmem)] * (len(pieces) + 2),
        out_specs=pl.BlockSpec(memory_space=vmem),
        scratch_shapes=[
            pltpu.VMEM((depth + 4, height + 4, in_count, width), jnp.bfloat16),
            pltpu.VMEM((depth + 2, height + 2, mid_count, width), jnp.bfloat16),
        ],
    )(keep, place, *pieces, w1, w2)


def tap_matrices(filters):
    a, b, e, o, c = filters.shape
    return filters.transpose(2, 3, 0, 1, 4).reshape(e * o, a * b * c)


def inside_flags(depth_rows, height_rows):
    tile_row, depth_tile, grid_depth = tile_place()
    d = lax.broadcasted_iota(jnp.int32, (depth_rows, height_rows), 0)
    h = lax.broadcasted_iota(jnp.int32, (depth_rows, height_rows), 1)
    keep = (d > 0) | (depth_tile > 0)
    keep &= (d < depth_rows - 1) | (depth_tile < grid_depth - 1)
    keep &= (h > 0) | (tile_row > 0)
    keep &= (h < height_rows - 1) | (tile_row < GH - 1)
    return keep.astype(jnp.int32).reshape(-1)


def gathered_filters(first_filters, second_filters):
    count = lax.axis_size("chan")
    own = lax.axis_index("chan")
    a, b, e, block, c = first_filters.shape
    own_block = first_filters.transpose(2, 3, 0, 1, 4).reshape(e, block, a * b * c)
    pieces = [own_block]
    for steps in range(1, count):
        pieces.append(passed_along(own_block, "chan", -steps))
    all_first = jnp.concatenate(pieces, 1).reshape(e * block * count, a * b * c)
    doubled = jnp.concatenate([second_filters, second_filters], 4)
    all_second = lax.dynamic_slice_in_dim(doubled, own * block, second_filters.shape[4], 4)
    return all_first, all_second


def local(voxels, first_filters, second_filters):
    place, pieces = halo_pieces(voxels, 2)
    all_first, second_filters = gathered_filters(first_filters, second_filters)
    keep = inside_flags(voxels.shape[1] + 2, voxels.shape[2] + 2)
    out = two_layers(keep, place, pieces, all_first, tap_matrices(second_filters))
    return out


def solution(mesh):
    return jax.shard_map(
        local,
        mesh=mesh,
        in_specs=(
            P(None, "space", None, None),
            P(None, None, None, "chan", None),
            P(None, None, None, "chan", None),
        ),
        out_specs=P("chan", "space", None, None),
        check_vma=False,
    )
```
